256 devices in a mesh: section: 16 (over z_lo, y, core), tensor: 16 (over x, z_hi).
Axes of the slice: x: 4, y: 4, z: 8 (z_hi: 4, z_lo: 2; z = z_hi * 2 + z_lo), core: 2. Of those that a mesh axis runs over, the one named last changes fastest.
Arguments:
- hidden: bfloat16 [16, 64, 8192], P('section'), may hold values from -14 to 14
- head: bfloat16 [8192, 65536], P('section', 'tensor'), may hold values from -0.25 to 0.25
- exit_loss_weight: float32 [16], P('section'), may hold values from 2 to 32
Outputs:
- grad_hidden: float32 [1024, 8192], P('tensor', 'section')
- grad_head: bfloat16 [8192, 65536], P('section', 'tensor')
The draws below stay inside these ranges and needn't reach their ends.
All inputs are finite; a program needn't handle non-finite values.
Results may differ from the reference program's by a relative error of at most 0.011.
Values may be sent and summed in bfloat16 or wider, within the bound.
No kernel may reach another device: no remote copies, remote signals or barrier semaphores. Data moves between devices by JAX's collectives and lax.ppermute only.
A program may use at most 128 MiB of HBM per device.

```python
import math
import jax
import jax.numpy as jnp
from jax import lax

D = 8192
TOK = 64
EXITS = 16
VOCAB = 65536


def head_block(key, index):
    base = jax.random.fold_in(jax.random.fold_in(key, 71), index)
    quantities = jnp.clip(jax.random.normal(base, (D, 128), jnp.float32), -6.0, 6.0)
    return quantities * (2.0 / math.sqrt(D))


def draw_head(key, part):
    blocks = lax.map(lambda index: head_block(key, index), jnp.arange(VOCAB // 128))
    return jnp.transpose(blocks, (1, 0, 2)).reshape(D, VOCAB).astype(jnp.bfloat16)


def draw_hidden(key, part):
    first_key = jax.random.fold_in(key, 13)
    base = jnp.clip(jax.random.normal(first_key, (EXITS, TOK, D), jnp.float32), -6.0, 6.0)
    return base.astype(jnp.bfloat16)


def steps_of(rng, extent, cuts, smallest, largest):
    gain = 1.0
    for dim, parts in cuts:
        draws = jax.random.uniform(jax.random.fold_in(jax.random.fold_in(rng, 6), dim), (parts,), jnp.float32, smallest / len(cuts), largest / len(cuts))
        gain = gain * jnp.repeat(jnp.exp(draws), extent[dim] // parts).reshape((-1,) + (1,) * (len(extent) - 1 - dim))
    return gain


def setup_inputs(seed: int = 0) -> dict:
    seeds = jax.random.split(jax.random.key(seed), 4)
    return {
        "hidden": draw_hidden(jax.random.fold_in(seeds[3], 71), 0),
        "head": draw_head(jax.random.fold_in(seeds[3], 71), 0),
        "exit_loss_weight": jnp.clip(jnp.exp(math.log(32.0) - 2.7725887 * jax.random.uniform(seeds[2], (EXITS,), jnp.float32) ** steps_of(seeds[2], (EXITS,), ((0, 16),), -0.2, 0.2)), 2.0, 32.0),
    }


scaling_divisor = 2.0


def reference(hidden, head, exit_loss_weight):
    departure_number, tok_count, width = hidden.shape
    row_total = departure_number * tok_count
    flat_hidden = hidden.reshape(row_total, width)
    lexicon_score_matrix = jnp.dot(flat_hidden, head, preferred_element_type=jnp.float32).reshape(departure_number, tok_count, -1)
    mentor_distribution = lexicon_score_matrix[departure_number - 1] / scaling_divisor
    log_student = lexicon_score_matrix - jax.nn.logsumexp(lexicon_score_matrix, axis=-1, keepdims=True)
    log_teacher = mentor_distribution - jax.nn.logsumexp(mentor_distribution, axis=-1, keepdims=True)
    log_mixture = jnp.logaddexp(log_student, log_teacher[None]) - jnp.log(2.0)
    midpoint_difference = 0.5 * (log_student - log_mixture)
    student = jnp.exp(log_student)
    average = jnp.sum(student * midpoint_difference, axis=-1, keepdims=True)
    grad_logits = (exit_loss_weight[:, None, None] * student * (midpoint_difference - average)).astype(jnp.bfloat16)
    grad_logits = grad_logits.reshape(row_total, -1)
    grad_head = jnp.dot(flat_hidden.T, grad_logits, preferred_element_type=jnp.float32).astype(jnp.bfloat16)
    grad_hidden = jnp.dot(grad_logits, head.T, preferred_element_type=jnp.float32)
    return grad_hidden, grad_head
```

```python
import math

import jax
import jax.numpy as jnp
from jax import lax
from jax.sharding import PartitionSpec as P

scaling_divisor = 2.0


def _lse(x, axes):
    top = jnp.max(x, axis=axes, keepdims=True)
    return top + jnp.log(jnp.sum(jnp.exp(x - top), axis=axes, keepdims=True))


def local(hidden, head, exit_loss_weight):
    sections = lax.axis_size("section")
    tensors = lax.axis_size("tensor")
    _, tok, width = hidden.shape
    exits = sections
    dblk = width // sections
    vblk = head.shape[1]
    tps = tok // sections
    n_eq = tensors // tps
    kpe = exits // n_eq

    x = hidden[0].reshape(tok, sections, dblk).transpose(1, 0, 2)
    cols = lax.all_to_all(x, "section", 0, 0, tiled=True)
    lhs = cols.reshape(exits, sections, tps, dblk).transpose(1, 0, 2, 3)
    lhs = lhs.reshape(sections * exits * tps, dblk)
    part = jnp.dot(lhs, head, preferred_element_type=jnp.float32)
    own = lax.psum_scatter(part, "section", scatter_dimension=0, tiled=True)
    own = own.reshape(n_eq, kpe, tps, vblk)
    stud = own.transpose(2, 0, 1, 3).reshape(tensors, kpe, vblk)
    teach = jnp.broadcast_to(own[n_eq - 1, kpe - 1][:, None, None, :], (tps, n_eq, 1, vblk))
    send = jnp.concatenate([stud, teach.reshape(tensors, 1, vblk)], axis=1)
    rows = lax.all_to_all(send, "tensor", 0, 0, tiled=True)

    logits = rows[:, :kpe, :]
    teacher = rows[:, kpe, :] / scaling_divisor
    log_student = logits - _lse(logits, (0, 2))
    log_teacher = teacher - _lse(teacher, (0, 1))
    log_mixture = jnp.logaddexp(log_student, log_teacher[:, None, :]) - jnp.log(2.0)
    halfgap = 0.5 * (log_student - log_mixture)
    student = jnp.exp(log_student)
    average = jnp.sum(student * halfgap, axis=(0, 2), keepdims=True)

    weights = lax.all_gather(exit_loss_weight, "section", axis=0, tiled=True)
    eq = lax.rem(lax.axis_index("tensor"), n_eq)
    wk = lax.dynamic_slice(weights, (eq * kpe,), (kpe,))
    grad_logits = (wk[None, :, None] * student * (halfgap - average)).astype(jnp.bfloat16)

    back = lax.all_to_all(grad_logits, "tensor", 0, 0, tiled=True)
    back = back.reshape(tps, exits, vblk)
    piece = lax.all_gather(back, "section", axis=0, tiled=True)

    head_grad = lax.dot_general(
        cols, piece, (((0, 1), (1, 0)), ((), ())), preferred_element_type=jnp.float32
    )
    row_grad = lax.dot_general(
        piece, head, (((2,), (1,)), ((), ())), preferred_element_type=jnp.float32
    )
    grad_hidden = lax.psum_scatter(row_grad, "tensor", scatter_dimension=1, tiled=True)
    grad_hidden = grad_hidden.reshape(tok, dblk)
    return (grad_hidden, head_grad.astype(jnp.bfloat16))


def solution(mesh):
    placed = (P("section", None, None), P("section", "tensor"), P("section"))
    return jax.shard_map(
        local,
        mesh=mesh,
        in_specs=placed,
        out_specs=(P("tensor", "section"), P("section", "tensor")),
        check_vma=False,
    )
```

```python
import jax
import jax.numpy as jnp
import numpy as np
from jax import lax
from jax.sharding import Mesh
from jax.sharding import PartitionSpec as P

scaling_divisor = 2.0
SEC = ("pair", "core")


def _lse(x, axes):
    top = jnp.max(x, axis=axes, keepdims=True)
    return top + jnp.log(jnp.sum(jnp.exp(x - top), axis=axes, keepdims=True))


def local(hidden, head, exit_loss_weight):
    pairs = lax.axis_size("pair")
    sections = pairs * 2
    tensors = lax.axis_size("tensor")
    _, tok, width = hidden.shape
    exits = sections
    dblk = width // sections
    vblk = head.shape[1]
    tps = tok // sections
    n_eq = tensors // tps
    kpe = exits // n_eq

    partner_head = lax.ppermute(head, "core", perm=[(0, 1), (1, 0)])
    head_pair = jnp.concatenate([head, partner_head], axis=0)

    h6 = hidden[0].reshape(pairs, 2, tps, pairs, 2, dblk)
    a = h6.transpose(3, 1, 0, 2, 4, 5)
    fwd = jnp.stack([a[:, 0], a[:, 1, :, :, ::-1, :]], axis=1)
    full = hidden[0].reshape(tok, sections, dblk).transpose(1, 0, 2)
    send = jnp.stack(
        [fwd.reshape(sections, -1), full.reshape(sections, -1)], axis=1
    )
    recv = lax.all_to_all(send, SEC, 0, 0, tiled=True)
    cols = recv[:, 1].reshape(exits, tok, dblk)
    lhs = recv[:, 0].reshape(exits, pairs, tps, 2 * dblk).transpose(1, 0, 2, 3)
    lhs = lhs.reshape(pairs * exits * tps, 2 * dblk)
    part = jnp.dot(lhs, head_pair, preferred_element_type=jnp.float32)
    part, w_local = lax.optimization_barrier((part, exit_loss_weight))
    weights = lax.all_gather(w_local, SEC, axis=0, tiled=True)
    own = lax.psum_scatter(part, "pair", scatter_dimension=0, tiled=True)
    own, weights = lax.optimization_barrier((own, weights))
    own = own.reshape(n_eq, kpe, tps, vblk)
    stud = own.transpose(2, 0, 1, 3).reshape(tensors, kpe, vblk)
    teach = jnp.broadcast_to(own[n_eq - 1, kpe - 1][:, None, None, :], (tps, n_eq, 1, vblk))
    send2 = jnp.concatenate([stud, teach.reshape(tensors, 1, vblk)], axis=1)
    rows = lax.all_to_all(send2, "tensor", 0, 0, tiled=True)

    logits = rows[:, :kpe, :]
    teacher = rows[:, kpe, :] / scaling_divisor
    log_student = logits - _lse(logits, (0, 2))
    log_teacher = teacher - _lse(teacher, (0, 1))
    log_mixture = jnp.logaddexp(log_student, log_teacher[:, None, :]) - jnp.log(2.0)
    halfgap = 0.5 * (log_student - log_mixture)
    student = jnp.exp(log_student)
    average = jnp.sum(student * halfgap, axis=(0, 2), keepdims=True)

    eq = lax.rem(lax.axis_index("tensor"), n_eq)
    wk = lax.dynamic_slice(weights, (eq * kpe,), (kpe,))
    grad_logits = (wk[None, :, None] * student * (halfgap - average)).astype(jnp.bfloat16)

    back = lax.all_to_all(grad_logits, "tensor", 0, 0, tiled=True)
    back = back.reshape(tps, exits, vblk)
    piece = lax.all_gather(back, SEC, axis=0, tiled=True)

    head_grad = lax.dot_general(
        cols, piece, (((0, 1), (1, 0)), ((), ())), preferred_element_type=jnp.float32
    )
    row_grad = lax.dot_general(
        piece, head, (((2,), (1,)), ((), ())), preferred_element_type=jnp.float32
    )
    grad_hidden = lax.psum_scatter(row_grad, "tensor", scatter_dimension=1, tiled=True)
    grad_hidden = grad_hidden.reshape(tok, dblk)
    return (grad_hidden, head_grad.astype(jnp.bfloat16))


def solution(mesh):
    shape = mesh.devices.shape
    inner = Mesh(
        np.asarray(mesh.devices).reshape(shape[0] // 2, 2, shape[1]), ("pair", "core", "tensor")
    )
    placed = (P(SEC, None, None), P(SEC, "tensor"), P(SEC))
    return jax.shard_map(
        local,
        mesh=inner,
        in_specs=placed,
        out_specs=(P("tensor", SEC), P(SEC, "tensor")),
        check_vma=False,
    )
```

```python
import math

import jax
import jax.numpy as jnp
from jax import lax
from jax.sharding import PartitionSpec as P

scaling_divisor = 2.0


def _lse(x, axes):
    top = jnp.max(x, axis=axes, keepdims=True)
    return top + jnp.log(jnp.sum(jnp.exp(x - top), axis=axes, keepdims=True))


def local(hidden, head, exit_loss_weight):
    sections = lax.axis_size("section")
    tensors = lax.axis_size("tensor")
    _, tok, width = hidden.shape
    exits = sections
    dblk = width // sections
    vblk = head.shape[1]
    tps = tok // sections
    n_eq = tensors // tps
    kpe = exits // n_eq

    x = hidden[0].reshape(tok, sections, dblk).transpose(1, 0, 2)
    cols = lax.all_to_all(x, "section", 0, 0, tiled=True)
    lhs = cols.reshape(exits, sections, tps, dblk).transpose(1, 0, 2, 3)
    lhs = lhs.reshape(sections * exits * tps, dblk)
    part = jnp.dot(lhs, head, preferred_element_type=jnp.float32)
    part, w_local = lax.optimization_barrier((part, exit_loss_weight))
    weights = lax.all_gather(w_local, "section", axis=0, tiled=True)
    own = lax.psum_scatter(part, "section", scatter_dimension=0, tiled=True)
    own, weights = lax.optimization_barrier((own, weights))
    own = own.reshape(n_eq, kpe, tps, vblk)
    stud = own.transpose(2, 0, 1, 3).reshape(tensors, kpe, vblk)
    teach = jnp.broadcast_to(own[n_eq - 1, kpe - 1][:, None, None, :], (tps, n_eq, 1, vblk))
    send = jnp.concatenate([stud, teach.reshape(tensors, 1, vblk)], axis=1)
    rows = lax.all_to_all(send, "tensor", 0, 0, tiled=True)

    logits = rows[:, :kpe, :]
    teacher = rows[:, kpe, :] / scaling_divisor
    log_student = logits - _lse(logits, (0, 2))
    log_teacher = teacher - _lse(teacher, (0, 1))
    log_mixture = jnp.logaddexp(log_student, log_teacher[:, None, :]) - jnp.log(2.0)
    halfgap = 0.5 * (log_student - log_mixture)
    student = jnp.exp(log_student)
    average = jnp.sum(student * halfgap, axis=(0, 2), keepdims=True)

    eq = lax.rem(lax.axis_index("tensor"), n_eq)
    wk = lax.dynamic_slice(weights, (eq * kpe,), (kpe,))
    grad_logits = (wk[None, :, None] * student * (halfgap - average)).astype(jnp.bfloat16)

    back = lax.all_to_all(grad_logits, "tensor", 0, 0, tiled=True)
    back = back.reshape(tps, exits, vblk).transpose(1, 0, 2)
    piece = lax.all_gather(back, "section", axis=1, tiled=True)

    head_grad = lax.dot_general(
        cols, piece, (((0, 1), (0, 1)), ((), ())), preferred_element_type=jnp.float32
    )
    row_grad = lax.dot_general(
        piece, head, (((2,), (1,)), ((), ())), preferred_element_type=jnp.float32
    )
    parts = lax.all_to_all(row_grad, "tensor", 0, 0, tiled=True)
    grad_hidden = jnp.sum(parts, axis=0)
    return (grad_hidden, head_grad.astype(jnp.bfloat16))


def solution(mesh):
    placed = (P("section", None, None), P("section", "tensor"), P("section"))
    return jax.shard_map(
        local,
        mesh=mesh,
        in_specs=placed,
        out_specs=(P("tensor", "section"), P("section", "tensor")),
        check_vma=False,
    )
```

```python
import jax
import jax.numpy as jnp
from jax import lax
from jax.sharding import PartitionSpec as P

scaling_divisor = 2.0
NCHUNK = 2


def _lse(x, axes):
    top = jnp.max(x, axis=axes, keepdims=True)
    return top + jnp.log(jnp.sum(jnp.exp(x - top), axis=axes, keepdims=True))


def local(hidden, head, exit_loss_weight):
    sections = lax.axis_size("section")
    tensors = lax.axis_size("tensor")
    _, tok, width = hidden.shape
    exits = sections
    dblk = width // sections
    vblk = head.shape[1]
    tps = tok // sections
    tpc = tps // NCHUNK
    n_eq = tensors // tpc
    kpe = exits // n_eq

    x = hidden[0].reshape(tok, sections, dblk).transpose(1, 0, 2)
    cols = lax.all_to_all(x, "section", 0, 0, tiled=True)
    cols4 = cols.reshape(exits, sections, tps, dblk)

    eq = lax.rem(lax.axis_index("tensor"), n_eq)
    parts = []
    for c in range(NCHUNK):
        sub = cols4[:, :, c * tpc:(c + 1) * tpc, :]
        lhs = sub.transpose(1, 0, 2, 3).reshape(sections * exits * tpc, dblk)
        parts.append(jnp.dot(lhs, head, preferred_element_type=jnp.float32))
    first, w_local = lax.optimization_barrier((parts[0], exit_loss_weight))
    parts[0] = first
    weights = lax.all_gather(w_local, "section", axis=0, tiled=True)
    owns = [lax.psum_scatter(p, "section", scatter_dimension=0, tiled=True) for p in parts]
    owns[0], weights = lax.optimization_barrier((owns[0], weights))

    pieces = []
    prev = None
    for c in range(NCHUNK):
        own = owns[c]
        if prev is not None:
            own, prev = lax.optimization_barrier((own, prev))
        own = own.reshape(n_eq, kpe, tpc, vblk)
        stud = own.transpose(2, 0, 1, 3).reshape(tensors, kpe, vblk)
        teach = jnp.broadcast_to(own[n_eq - 1, kpe - 1][:, None, None, :], (tpc, n_eq, 1, vblk))
        send = jnp.concatenate([stud, teach.reshape(tensors, 1, vblk)], axis=1)
        rows = lax.all_to_all(send, "tensor", 0, 0, tiled=True)

        logits = rows[:, :kpe, :]
        teacher = rows[:, kpe, :] / scaling_divisor
        log_student = logits - _lse(logits, (0, 2))
        log_teacher = teacher - _lse(teacher, (0, 1))
        log_mixture = jnp.logaddexp(log_student, log_teacher[:, None, :]) - jnp.log(2.0)
        halfgap = 0.5 * (log_student - log_mixture)
        student = jnp.exp(log_student)
        average = jnp.sum(student * halfgap, axis=(0, 2), keepdims=True)
        wk = lax.dynamic_slice(weights, (eq * kpe,), (kpe,))
        grad_logits = (wk[None, :, None] * student * (halfgap - average)).astype(jnp.bfloat16)

        back = lax.all_to_all(grad_logits, "tensor", 0, 0, tiled=True)
        prev = back
        back = back.reshape(tpc, exits, vblk).transpose(1, 0, 2)
        pieces.append(lax.all_gather(back, "section", axis=1, tiled=True))

    head_grad = None
    row_grads = []
    for c in range(NCHUNK):
        piece = pieces[c]
        sub = cols4[:, :, c * tpc:(c + 1) * tpc, :].reshape(exits, sections * tpc, dblk)
        contrib = lax.dot_general(
            sub, piece, (((0, 1), (0, 1)), ((), ())), preferred_element_type=jnp.float32
        )
        head_grad = contrib if head_grad is None else head_grad + contrib
        row_grads.append(
            lax.dot_general(
                piece, head, (((2,), (1,)), ((), ())), preferred_element_type=jnp.float32
            ).reshape(exits, sections, tpc, dblk)
        )
    row_grad = jnp.stack(row_grads, axis=2).reshape(exits, tok, dblk)
    got = lax.all_to_all(row_grad, "tensor", 0, 0, tiled=True)
    grad_hidden = jnp.sum(got, axis=0)
    return (grad_hidden, head_grad.astype(jnp.bfloat16))


def solution(mesh):
    placed = (P("section", None, None), P("section", "tensor"), P("section"))
    return jax.shard_map(
        local,
        mesh=mesh,
        in_specs=placed,
        out_specs=(P("tensor", "section"), P("section", "tensor")),
        check_vma=False,
    )
```

```python
import math

import jax
import jax.numpy as jnp
from jax import lax
from jax.sharding import PartitionSpec as P

scaling_divisor = 2.0


def _lse(x, axes):
    top = jnp.max(x, axis=axes, keepdims=True)
    return top + jnp.log(jnp.sum(jnp.exp(x - top), axis=axes, keepdims=True))


def local(hidden, head, exit_loss_weight):
    sections = lax.axis_size("section")
    tensors = lax.axis_size("tensor")
    _, tok, width = hidden.shape
    exits = sections
    dblk = width // sections
    vblk = head.shape[1]
    tps = tok // sections
    n_eq = tensors // tps
    kpe = exits // n_eq

    x = hidden[0].reshape(tok, sections, dblk).transpose(1, 0, 2)
    cols = lax.all_to_all(x, "section", 0, 0, tiled=True)
    lhs = cols.reshape(exits, sections, tps, dblk).transpose(1, 0, 2, 3)
    lhs = lhs.reshape(sections * exits * tps, dblk)
    part = jnp.dot(lhs, head, preferred_element_type=jnp.float32)
    part, w_local = lax.optimization_barrier((part, exit_loss_weight))
    weights = lax.all_gather(w_local, "section", axis=0, tiled=True)
    own = lax.psum_scatter(part, "section", scatter_dimension=0, tiled=True)
    own, weights = lax.optimization_barrier((own, weights))
    own = own.reshape(n_eq, kpe, tps, vblk)
    stud = own.transpose(2, 0, 1, 3).reshape(tensors, kpe, vblk)
    teach = jnp.broadcast_to(own[n_eq - 1, kpe - 1][:, None, None, :], (tps, n_eq, 1, vblk))
    send = jnp.concatenate([stud, teach.reshape(tensors, 1, vblk)], axis=1)
    rows = lax.all_to_all(send, "tensor", 0, 0, tiled=True)

    logits = rows[:, :kpe, :]
    teacher = rows[:, kpe, :] / scaling_divisor
    log_student = logits - _lse(logits, (0, 2))
    log_teacher = teacher - _lse(teacher, (0, 1))
    log_mixture = jnp.logaddexp(log_student, log_teacher[:, None, :]) - jnp.log(2.0)
    halfgap = 0.5 * (log_student - log_mixture)
    student = jnp.exp(log_student)
    average = jnp.sum(student * halfgap, axis=(0, 2), keepdims=True)

    eq = lax.rem(lax.axis_index("tensor"), n_eq)
    wk = lax.dynamic_slice(weights, (eq * kpe,), (kpe,))
    grad_logits = (wk[None, :, None] * student * (halfgap - average)).astype(jnp.bfloat16)

    back = lax.all_to_all(grad_logits, "tensor", 0, 0, tiled=True)
    back = back.reshape(tps, exits, vblk).transpose(1, 0, 2)
    piece = lax.all_gather(back, "section", axis=1, tiled=True)

    head_grad = lax.dot_general(
        cols, piece, (((0, 1), (0, 1)), ((), ())), preferred_element_type=jnp.float32
    )
    row_grad = lax.dot_general(
        piece, head, (((2,), (1,)), ((), ())), preferred_element_type=jnp.float32
    )
    parts = lax.all_to_all(row_grad.astype(jnp.bfloat16), "tensor", 0, 0, tiled=True)
    grad_hidden = jnp.sum(parts.astype(jnp.float32), axis=0)
    return (grad_hidden, head_grad.astype(jnp.bfloat16))


def solution(mesh):
    placed = (P("section", None, None), P("section", "tensor"), P("section"))
    return jax.shard_map(
        local,
        mesh=mesh,
        in_specs=placed,
        out_specs=(P("tensor", "section"), P("section", "tensor")),
        check_vma=False,
    )
```

```python
import jax
import jax.numpy as jnp
from jax import lax
from jax.sharding import PartitionSpec as P

scaling_divisor = 2.0


def _gather_small(x, axis, count):
    sent = jnp.broadcast_to(x[None], (count,) + x.shape)
    return lax.all_to_all(sent, axis, 0, 0, tiled=True)


def local(hidden, head, exit_loss_weight):
    sections = lax.axis_size("section")
    tensors = lax.axis_size("tensor")
    _, tok, width = hidden.shape
    exits = sections
    dblk = width // sections
    vblk = head.shape[1]
    tps = tok // sections

    x = hidden[0].reshape(tok, sections, dblk).transpose(1, 0, 2)
    cols = lax.all_to_all(x, "section", 0, 0, tiled=True)
    lhs = cols.reshape(exits, sections, tps, dblk).transpose(1, 0, 2, 3)
    lhs = lhs.reshape(sections * exits * tps, dblk)
    part = jnp.dot(lhs, head, preferred_element_type=jnp.float32)
    part, w_local = lax.optimization_barrier((part, exit_loss_weight))
    weights = lax.all_gather(w_local, "section", axis=0, tiled=True)
    own = lax.psum_scatter(part, "section", scatter_dimension=0, tiled=True)
    own, weights = lax.optimization_barrier((own, weights))
    logits = own.reshape(exits, tps, vblk)
    teacher = logits[exits - 1] / scaling_divisor

    top_s = jnp.max(logits, axis=2)
    top_t = jnp.max(teacher, axis=1)
    sum_s = jnp.sum(jnp.exp(logits - top_s[:, :, None]), axis=2)
    sum_t = jnp.sum(jnp.exp(teacher - top_t[:, None]), axis=1)
    stats = jnp.stack(
        [jnp.concatenate([top_s.reshape(-1), top_t]), jnp.concatenate([sum_s.reshape(-1), sum_t])]
    )
    got = _gather_small(stats, "tensor", tensors)
    peak = jnp.max(got[:, 0], axis=0)
    norm = peak + jnp.log(jnp.sum(got[:, 1] * jnp.exp(got[:, 0] - peak[None]), axis=0))
    student_norm = norm[: exits * tps].reshape(exits, tps)
    teacher_norm = norm[exits * tps :]

    log_student = logits - student_norm[:, :, None]
    log_teacher = teacher - teacher_norm[:, None]
    log_mixture = jnp.logaddexp(log_student, log_teacher[None]) - jnp.log(2.0)
    halfgap = 0.5 * (log_student - log_mixture)
    student = jnp.exp(log_student)
    average = jnp.sum(_gather_small(jnp.sum(student * halfgap, axis=2), "tensor", tensors), axis=0)
    grad_logits = (
        weights[:, None, None] * student * (halfgap - average[:, :, None])
    ).astype(jnp.bfloat16)
    piece = lax.all_gather(grad_logits, "section", axis=1, tiled=True)

    head_grad = lax.dot_general(
        cols, piece, (((0, 1), (0, 1)), ((), ())), preferred_element_type=jnp.float32
    )
    row_grad = lax.dot_general(
        piece, head, (((2,), (1,)), ((), ())), preferred_element_type=jnp.float32
    )
    parts = lax.all_to_all(row_grad.astype(jnp.bfloat16), "tensor", 0, 0, tiled=True)
    grad_hidden = jnp.sum(parts.astype(jnp.float32), axis=0)
    return (grad_hidden, head_grad.astype(jnp.bfloat16))


def solution(mesh):
    placed = (P("section", None, None), P("section", "tensor"), P("section"))
    return jax.shard_map(
        local,
        mesh=mesh,
        in_specs=placed,
        out_specs=(P("tensor", "section"), P("section", "tensor")),
        check_vma=False,
    )
```

```python
import jax
import jax.numpy as jnp
from jax import lax
from jax.sharding import PartitionSpec as P

scaling_divisor = 2.0


def _gather_small(x, axis, count):
    sent = jnp.broadcast_to(x[None], (count,) + x.shape)
    return lax.all_to_all(sent, axis, 0, 0, tiled=True)


def local(hidden, head, exit_loss_weight):
    sections = lax.axis_size("section")
    tensors = lax.axis_size("tensor")
    _, tok, width = hidden.shape
    exits = sections
    dblk = width // sections
    vblk = head.shape[1]
    tps = tok // sections

    x = hidden[0].reshape(tok, sections, dblk).transpose(1, 0, 2)
    cols = lax.all_to_all(x, "section", 0, 0, tiled=True)
    lhs = cols.reshape(exits, sections, tps, dblk).transpose(1, 0, 2, 3)
    lhs = lhs.reshape(sections * exits * tps, dblk)
    part = jnp.dot(lhs, head, preferred_element_type=jnp.float32)
    part, w_local = lax.optimization_barrier((part, exit_loss_weight))
    weights = lax.all_gather(w_local, "section", axis=0, tiled=True)
    own = lax.psum_scatter(part, "section", scatter_dimension=0, tiled=True)
    own, weights = lax.optimization_barrier((own, weights))
    logits = own.reshape(exits, tps, vblk)
    teacher = logits[exits - 1] / scaling_divisor

    rows = jnp.concatenate([own, teacher], axis=0)
    top = jnp.max(rows, axis=1)
    shifted = jnp.exp(rows - top[:, None])
    stats = jnp.stack([top, jnp.sum(shifted, axis=1)])
    got = _gather_small(stats, "tensor", tensors)
    peak = jnp.max(got[:, 0], axis=0)
    norm = peak + jnp.log(jnp.sum(got[:, 1] * jnp.exp(got[:, 0] - peak[None]), axis=0))
    student_norm = norm[: exits * tps].reshape(exits, tps)
    teacher_norm = norm[exits * tps :]

    log_student = logits - student_norm[:, :, None]
    log_teacher = teacher - teacher_norm[:, None]
    log_mixture = jnp.logaddexp(log_student, log_teacher[None]) - jnp.log(2.0)
    halfgap = 0.5 * (log_student - log_mixture)
    scale = jnp.exp(top - norm)[: exits * tps].reshape(exits, tps)
    student = shifted[: exits * tps].reshape(exits, tps, vblk) * scale[:, :, None]
    average = jnp.sum(_gather_small(jnp.sum(student * halfgap, axis=2), "tensor", tensors), axis=0)
    grad_logits = (
        weights[:, None, None] * student * (halfgap - average[:, :, None])
    ).astype(jnp.bfloat16)
    piece = lax.all_gather(grad_logits, "section", axis=1, tiled=True)

    head_grad = lax.dot_general(
        cols, piece, (((0, 1), (0, 1)), ((), ())), preferred_element_type=jnp.float32
    )
    row_grad = lax.dot_general(
        piece, head, (((2,), (1,)), ((), ())), preferred_element_type=jnp.float32
    )
    parts = lax.all_to_all(row_grad.astype(jnp.bfloat16), "tensor", 0, 0, tiled=True)
    grad_hidden = jnp.sum(parts.astype(jnp.float32), axis=0)
    return (grad_hidden, head_grad.astype(jnp.bfloat16))


def solution(mesh):
    placed = (P("section", None, None), P("section", "tensor"), P("section"))
    return jax.shard_map(
        local,
        mesh=mesh,
        in_specs=placed,
        out_specs=(P("tensor", "section"), P("section", "tensor")),
        check_vma=False,
    )
```

```python
import jax
import jax.numpy as jnp
from jax import lax
from jax.sharding import PartitionSpec as P

scaling_divisor = 2.0


def _gather_small(x, axis, count):
    sent = jnp.broadcast_to(x[None], (count,) + x.shape)
    return lax.all_to_all(sent, axis, 0, 0, tiled=True)


def local(hidden, head, exit_loss_weight):
    sections = lax.axis_size("section")
    tensors = lax.axis_size("tensor")
    _, tok, width = hidden.shape
    exits = sections
    dblk = width // sections
    vblk = head.shape[1]
    tps = tok // sections

    x = hidden[0].reshape(tok, sections, dblk).transpose(1, 0, 2)
    cols = lax.all_to_all(x, "section", 0, 0, tiled=True)
    lhs = cols.reshape(exits, sections, tps, dblk).transpose(1, 0, 2, 3)
    lhs = lhs.reshape(sections * exits * tps, dblk)
    part = jnp.dot(lhs, head, preferred_element_type=jnp.float32)
    part, w_local = lax.optimization_barrier((part, exit_loss_weight))
    weights = lax.all_gather(w_local, "section", axis=0, tiled=True)
    own = lax.psum_scatter(part, "section", scatter_dimension=0, tiled=True)
    own, weights = lax.optimization_barrier((own, weights))
    logits = own.reshape(exits, tps, vblk)
    teacher = logits[exits - 1] / scaling_divisor

    rows = jnp.concatenate([own, teacher], axis=0)
    top = jnp.max(rows, axis=1)
    shifted = jnp.exp(rows - top[:, None])
    stats = jnp.stack([top, jnp.sum(shifted, axis=1)])
    got = _gather_small(stats, "tensor", tensors)
    peak = jnp.max(got[:, 0], axis=0)
    norm = peak + jnp.log(jnp.sum(got[:, 1] * jnp.exp(got[:, 0] - peak[None]), axis=0))
    student_norm = norm[: exits * tps].reshape(exits, tps)
    teacher_norm = norm[exits * tps :]

    gap = teacher[None] - logits
    delta = teacher_norm[None, :] - student_norm
    halfgap = 0.5 * jnp.log(2.0) - 0.5 * jax.nn.softplus(gap - delta[:, :, None])
    scale = jnp.exp(top - norm)[: exits * tps].reshape(exits, tps)
    student = shifted[: exits * tps].reshape(exits, tps, vblk) * scale[:, :, None]
    average = jnp.sum(_gather_small(jnp.sum(student * halfgap, axis=2), "tensor", tensors), axis=0)
    grad_logits = (
        weights[:, None, None] * student * (halfgap - average[:, :, None])
    ).astype(jnp.bfloat16)
    piece = lax.all_gather(grad_logits, "section", axis=1, tiled=True)

    head_grad = lax.dot_general(
        cols, piece, (((0, 1), (0, 1)), ((), ())), preferred_element_type=jnp.float32
    )
    row_grad = lax.dot_general(
        piece, head, (((2,), (1,)), ((), ())), preferred_element_type=jnp.float32
    )
    parts = lax.all_to_all(row_grad.astype(jnp.bfloat16), "tensor", 0, 0, tiled=True)
    grad_hidden = jnp.sum(parts.astype(jnp.float32), axis=0)
    return (grad_hidden, head_grad.astype(jnp.bfloat16))


def solution(mesh):
    placed = (P("section", None, None), P("section", "tensor"), P("section"))
    return jax.shard_map(
        local,
        mesh=mesh,
        in_specs=placed,
        out_specs=(P("tensor", "section"), P("section", "tensor")),
        check_vma=False,
    )
```

```python
import jax
import jax.numpy as jnp
from jax import lax
from jax.sharding import PartitionSpec as P

scaling_divisor = 2.0


def _gather_small(x, axis, count):
    sent = jnp.broadcast_to(x[None], (count,) + x.shape)
    return lax.all_to_all(sent, axis, 0, 0, tiled=True)


def local(hidden, head, exit_loss_weight):
    sections = lax.axis_size("section")
    tensors = lax.axis_size("tensor")
    _, tok, width = hidden.shape
    exits = sections
    dblk = width // sections
    vblk = head.shape[1]
    tps = tok // sections

    x = hidden[0].reshape(tok, sections, dblk).transpose(1, 0, 2)
    cols = lax.all_to_all(x, "section", 0, 0, tiled=True)
    lhs = cols.reshape(exits, sections, tps, dblk).transpose(1, 0, 2, 3)
    lhs = lhs.reshape(sections * exits * tps, dblk)
    part = jnp.dot(lhs, head, preferred_element_type=jnp.float32)
    part, w_local = lax.optimization_barrier((part, exit_loss_weight))
    weights = lax.all_gather(w_local, "section", axis=0, tiled=True)
    own = lax.psum_scatter(part, "section", scatter_dimension=0, tiled=True)
    own, weights = lax.optimization_barrier((own, weights))
    logits = own.reshape(exits, tps, vblk)
    teacher = logits[exits - 1] / scaling_divisor

    top_s = jnp.max(own, axis=1)
    top_t = top_s[(exits - 1) * tps:] / scaling_divisor
    shifted = jnp.exp(own - top_s[:, None])
    sum_t = jnp.sum(jnp.exp(teacher - top_t[:, None]), axis=1)
    top = jnp.concatenate([top_s, top_t])
    stats = jnp.stack([top, jnp.concatenate([jnp.sum(shifted, axis=1), sum_t])])
    got = _gather_small(stats, "tensor", tensors)
    peak = jnp.max(got[:, 0], axis=0)
    norm = peak + jnp.log(jnp.sum(got[:, 1] * jnp.exp(got[:, 0] - peak[None]), axis=0))
    student_norm = norm[: exits * tps].reshape(exits, tps)
    teacher_norm = norm[exits * tps :]

    gap = teacher[None] - logits
    delta = teacher_norm[None, :] - student_norm
    halfgap = 0.5 * jnp.log(2.0) - 0.5 * jax.nn.softplus(gap - delta[:, :, None])
    scale = jnp.exp(top - norm)[: exits * tps].reshape(exits, tps)
    student = shifted.reshape(exits, tps, vblk) * scale[:, :, None]
    average = jnp.sum(_gather_small(jnp.sum(student * halfgap, axis=2), "tensor", tensors), axis=0)
    grad_logits = (
        weights[:, None, None] * student * (halfgap - average[:, :, None])
    ).astype(jnp.bfloat16)
    piece = lax.all_gather(grad_logits, "section", axis=1, tiled=True)

    head_grad = lax.dot_general(
        cols, piece, (((0, 1), (0, 1)), ((), ())), preferred_element_type=jnp.float32
    )
    row_grad = lax.dot_general(
        piece, head, (((2,), (1,)), ((), ())), preferred_element_type=jnp.float32
    )
    parts = lax.all_to_all(row_grad.astype(jnp.bfloat16), "tensor", 0, 0, tiled=True)
    grad_hidden = jnp.sum(parts.astype(jnp.float32), axis=0)
    return (grad_hidden, head_grad.astype(jnp.bfloat16))


def solution(mesh):
    placed = (P("section", None, None), P("section", "tensor"), P("section"))
    return jax.shard_map(
        local,
        mesh=mesh,
        in_specs=placed,
        out_specs=(P("tensor", "section"), P("section", "tensor")),
        check_vma=False,
    )
```

```python
import jax
import jax.numpy as jnp
from jax import lax
from jax.sharding import PartitionSpec as P

scaling_divisor = 2.0


def _gather_small(x, axis, count):
    sent = jnp.broadcast_to(x[None], (count,) + x.shape)
    return lax.all_to_all(sent, axis, 0, 0, tiled=True)


def local(hidden, head, exit_loss_weight):
    sections = lax.axis_size("section")
    tensors = lax.axis_size("tensor")
    _, tok, width = hidden.shape
    exits = sections
    dblk = width // sections
    vblk = head.shape[1]
    tps = tok // sections

    x = hidden[0].reshape(tok, sections, dblk).transpose(1, 0, 2)
    cols = lax.all_to_all(x, "section", 0, 0, tiled=True)
    lhs = cols.reshape(exits, sections, tps, dblk).transpose(1, 0, 2, 3)
    lhs = lhs.reshape(sections * exits * tps, dblk)
    part = jnp.dot(lhs, head, preferred_element_type=jnp.float32)
    part, w_local = lax.optimization_barrier((part, exit_loss_weight))
    weights = lax.all_gather(w_local, "section", axis=0, tiled=True)
    own = lax.psum_scatter(part, "section", scatter_dimension=0, tiled=True)
    own, weights = lax.optimization_barrier((own, weights))
    logits = own.reshape(exits, tps, vblk)
    teacher = logits[exits - 1] / scaling_divisor

    rows = jnp.concatenate([own, teacher], axis=0)
    top = jnp.max(rows, axis=1)
    shifted = jnp.exp(rows - top[:, None])
    stats = jnp.stack([top, jnp.sum(shifted, axis=1)])
    got = _gather_small(stats, "tensor", tensors)
    peak = jnp.max(got[:, 0], axis=0)
    norm = peak + jnp.log(jnp.sum(got[:, 1] * jnp.exp(got[:, 0] - peak[None]), axis=0))
    student_norm = norm[: exits * tps].reshape(exits, tps)
    teacher_norm = norm[exits * tps :]

    gap = teacher[None] - logits
    delta = teacher_norm[None, :] - student_norm
    halfgap = 0.5 * jnp.log(2.0) - 0.5 * jax.nn.softplus(gap - delta[:, :, None])
    scale = jnp.exp(top - norm)[: exits * tps].reshape(exits, tps)
    student = shifted[: exits * tps].reshape(exits, tps, vblk) * scale[:, :, None]
    weighted = weights[:, None, None] * student
    lead = weighted * halfgap
    partial_average = jnp.sum(student * halfgap, axis=2)
    lead, weighted, partial_average = lax.optimization_barrier((lead, weighted, partial_average))
    average = jnp.sum(_gather_small(partial_average, "tensor", tensors), axis=0)
    grad_logits = (lead - average[:, :, None] * weighted).astype(jnp.bfloat16)
    piece = lax.all_gather(grad_logits, "section", axis=1, tiled=True)

    head_grad = lax.dot_general(
        cols, piece, (((0, 1), (0, 1)), ((), ())), preferred_element_type=jnp.float32
    )
    row_grad = lax.dot_general(
        piece, head, (((2,), (1,)), ((), ())), preferred_element_type=jnp.float32
    )
    parts = lax.all_to_all(row_grad.astype(jnp.bfloat16), "tensor", 0, 0, tiled=True)
    grad_hidden = jnp.sum(parts.astype(jnp.float32), axis=0)
    return (grad_hidden, head_grad.astype(jnp.bfloat16))


def solution(mesh):
    placed = (P("section", None, None), P("section", "tensor"), P("section"))
    return jax.shard_map(
        local,
        mesh=mesh,
        in_specs=placed,
        out_specs=(P("tensor", "section"), P("section", "tensor")),
        check_vma=False,
    )
```
